512 devices in a mesh: tm: 64 (over z, y_hi, core), space: 8 (over y_lo, x).
Axes of the slice: x: 4, y: 4 (y_hi: 2, y_lo: 2; y = y_hi * 2 + y_lo), z: 16, core: 2. Of those that a mesh axis runs over, the one named last changes fastest.
Arguments:
- start_states: float32 [64, 256, 256], P('tm', 'space'), may hold values from -6 to 6
- region_map: int32 [256, 256], P('space'), may hold values from 0 to 3
- source: float32 [2, 256, 256], P(None, 'space'), may hold values from -6 to 6
- front: int32 [], replicated, may hold values from 33 to 63
Outputs:
- new_states: float32 [64, 256, 256], P('tm', 'space')
- jumps: float32 [64, 256, 256], P('tm', 'space')
The draws below stay inside these ranges and needn't reach their ends.
All inputs are finite; a program needn't handle non-finite values.
Results may differ from the reference program's by a relative error of at most 0.000027.
Values sent between devices are 32-bit elements; how exact they have to be, the bound alone decides.
No kernel may reach another device: no remote copies, remote signals or barrier semaphores. Data moves between devices by JAX's collectives and lax.ppermute only.
A program may use at most 64 MiB of HBM per device.

```python
import math
import jax
import jax.numpy as jnp
from jax import lax

NC = 256
FINE = 16
ITERS = 2
SLICES = 64
NR = 256


def place_ends(array, own_key, smallest, high):
    place = [jax.random.randint(jax.random.fold_in(own_key, axis), (), 0, length) for axis, length in enumerate(array.shape)]
    longest = array.shape.index(max(array.shape))
    neighbour = place[:longest] + [(place[longest] + 1) % array.shape[longest]] + place[longest + 1:]
    return array.at[tuple(place)].set(smallest).at[tuple(neighbour)].set(high)


def shard_levels(own_key, dims, split, smallest, top_value):
    factor_of = 1.0
    for position, shards_of in split:
        draws = jax.random.uniform(jax.random.fold_in(jax.random.fold_in(own_key, 6), position), (shards_of,), jnp.float32, smallest / len(split), top_value / len(split))
        factor_of = factor_of * jnp.repeat(jnp.exp(draws), dims[position] // shards_of).reshape((-1,) + (1,) * (len(dims) - 1 - position))
    return factor_of


def noise(stream_key, dims, width, reach, split=(), kind=jnp.bfloat16):
    drawn = width * jax.random.normal(stream_key, dims, jnp.float32)
    if split:
        drawn = drawn * shard_levels(stream_key, dims, split, -0.22, 0.18)
    return jnp.clip(drawn, -reach, reach).astype(kind)


def setup_inputs(seed: int = 0) -> dict:
    key_of = jax.random.split(jax.random.key(seed), 5)
    return {
        "start_states": noise(key_of[0], (SLICES, NR, NC), 1.0, 6.0, ((0, 64), (1, 8)), jnp.float32),
        "region_map": place_ends(jax.random.randint(key_of[1], (NR, NC), 0, 4), jax.random.fold_in(key_of[1], 1), 0, 3).astype(jnp.int32),
        "source": noise(key_of[2], (2, NR, NC), 1.0, 6.0, ((1, 8),), jnp.float32),
        "front": jax.random.randint(key_of[3], (), SLICES // 2 + 1, SLICES).astype(jnp.int32),
    }


RELUCTIVITY = (1.0, 0.3, 1.0, 0.25)
SATURATION = (0.0, 2.0, 0.0, 1.5)
MOBILITY = (0.15, 0.02, 0.0004, 0.0008)


def lookup(region_map, table):
    result = jnp.zeros(region_map.shape, jnp.float32)
    for region, entry_value in enumerate(table):
        result = result + jnp.where(region_map == region, jnp.float32(entry_value), jnp.float32(0.0))
    return result


def flux_terms(extended, reluctivity, saturation):
    field_cols = jnp.pad(extended, ((0, 0), (1, 1)))
    relu_cols = jnp.pad(reluctivity, ((0, 0), (1, 1)))
    satu_cols = jnp.pad(saturation, ((0, 0), (1, 1)))
    center = field_cols[1:-1, 1:-1]
    own_rel = relu_cols[1:-1, 1:-1]
    own_sat = satu_cols[1:-1, 1:-1]
    divergence = jnp.zeros_like(center)
    diagonal = jnp.zeros_like(center)
    for row_part, col_part in ((slice(0, -2), slice(1, -1)), (slice(2, None), slice(1, -1)), (slice(1, -1), slice(0, -2)), (slice(1, -1), slice(2, None))):
        difference = field_cols[row_part, col_part] - center
        square = difference * difference
        face_rel = 0.5 * (own_rel + relu_cols[row_part, col_part])
        face_sat = 0.5 * (own_sat + satu_cols[row_part, col_part])
        weight = face_rel * (1.0 + face_sat * square / (1.0 + square))
        divergence = divergence + weight * difference
        diagonal = diagonal + weight
    return divergence, diagonal


def compose_maps(earlier, later):
    return (later[0] * earlier[0], later[0] * earlier[1] + later[1])


def reference(start_states, region_map, source, front):
    reluct = lookup(region_map, RELUCTIVITY)
    satur = lookup(region_map, SATURATION)
    mobile = lookup(region_map, MOBILITY)
    padded_rel = jnp.pad(reluct, ((1, 1), (0, 0)))
    padded_sat = jnp.pad(satur, ((1, 1), (0, 0)))
    scale = 2.0 * math.pi / (SLICES * FINE)

    def fine_solve(inputs):
        field_now, slice_index = inputs
        first_diag = jnp.zeros_like(field_now)
        for step_index in range(FINE):
            extended = jnp.pad(field_now, ((1, 1), (0, 0)))
            divergence, diagonal = flux_terms(extended, padded_rel, padded_sat)
            if step_index == 0:
                first_diag = diagonal
            phase_angle = (slice_index * FINE + step_index).astype(jnp.float32) * scale
            current = source[0] * jnp.cos(phase_angle) + source[1] * jnp.sin(phase_angle)
            field_now = field_now + mobile * (divergence + current)
        return field_now, first_diag

    indices = jnp.arange(SLICES, dtype=jnp.int32)
    cut_slice = (front - 1) % SLICES
    states = start_states
    fine_ends = start_states
    for sweep in range(ITERS):
        fine_ends, diagonals = lax.map(fine_solve, (states, indices))
        decay = 1.0 / (1.0 + FINE * mobile * diagonals)
        decay = jnp.where((indices != cut_slice)[:, None, None], decay, 0.0)
        offset = fine_ends - decay * states

        def compose_step(carry, element):
            joined = compose_maps(carry, element)
            return joined, joined

        unit = (jnp.ones_like(mobile), jnp.zeros_like(mobile))
        final_pair, inclusive = lax.scan(compose_step, unit, (decay, offset))
        incl_decay, incl_offset = inclusive
        closing = incl_offset[-1]
        excl_decay = jnp.concatenate([jnp.ones_like(closing)[None], incl_decay[:-1]], 0)
        excl_offset = jnp.concatenate([jnp.zeros_like(closing)[None], incl_offset[:-1]], 0)
        states = excl_decay * closing + excl_offset
    jumps = jnp.roll(fine_ends, 1, axis=0) - states
    return (states, jumps)
```

```python
import math

import jax
import jax.numpy as jnp
from jax import lax
from jax.sharding import PartitionSpec as P

FINE = 16
ITERS = 2
SCAN_RADIX = 4


RELUCTIVITY = (1.0, 0.3, 1.0, 0.25)
SATURATION = (0.0, 2.0, 0.0, 1.5)
MOBILITY = (0.15, 0.02, 0.0004, 0.0008)


def with_halo(block, width):
    count = lax.axis_size("space")
    rows = block.shape[-2]
    forward = [(i, i + 1) for i in range(count - 1)]
    backward = [(i + 1, i) for i in range(count - 1)]
    above = lax.ppermute(lax.slice_in_dim(block, rows - width, rows, axis=block.ndim - 2), "space", forward)
    below = lax.ppermute(lax.slice_in_dim(block, 0, width, axis=block.ndim - 2), "space", backward)
    return jnp.concatenate([above, block, below], axis=block.ndim - 2)


def lookup_shifted(code, table):
    result = jnp.zeros(code.shape, jnp.float32)
    for region, entry_value in enumerate(table):
        result = result + jnp.where(code == jnp.float32(region + 1), jnp.float32(entry_value), jnp.float32(0.0))
    return result


def face_terms(values, axis):
    pad = [(0, 0)] * values.ndim
    pad[axis] = (1, 1)
    padded = jnp.pad(values, pad)
    n = padded.shape[axis]
    return 0.5 * (lax.slice_in_dim(padded, 0, n - 1, axis=axis) + lax.slice_in_dim(padded, 1, n, axis=axis))


def flux_terms(field, row_rel, row_sat, col_rel, col_sat):
    rows, cols = field.shape
    rpad = jnp.pad(field, ((1, 1), (0, 0)))
    row_diff = rpad[1:] - rpad[:-1]
    row_sq = row_diff * row_diff
    row_w = row_rel * (1.0 + row_sat * row_sq / (1.0 + row_sq))
    row_flux = row_w * row_diff
    cpad = jnp.pad(field, ((0, 0), (1, 1)))
    col_diff = cpad[:, 1:] - cpad[:, :-1]
    col_sq = col_diff * col_diff
    col_w = col_rel * (1.0 + col_sat * col_sq / (1.0 + col_sq))
    col_flux = col_w * col_diff
    divergence = (((-row_flux[:-1]) + row_flux[1:]) + (-col_flux[:, :-1])) + col_flux[:, 1:]
    diagonal = ((row_w[:-1] + row_w[1:]) + col_w[:, :-1]) + col_w[:, 1:]
    return divergence, diagonal


def compose_maps(earlier, later):
    return (later[0] * earlier[0], later[0] * earlier[1] + later[1])


def periodic_states(decay, offset, extra):
    count = lax.axis_size("tm")

    def from_behind(x, by):
        return lax.ppermute(x, "tm", [(i, (i + by) % count) for i in range(count)])

    own = jnp.stack([decay, offset])
    first = min(SCAN_RADIX, count)
    got = [from_behind(jnp.stack([decay, offset] + extra), 1)]
    got += [from_behind(own, by) for by in range(2, first + 1)]
    carried = [part[2:] for part in got[:1]]
    window = (got[-1][0], got[-1][1])
    for part in reversed(got[:-1]):
        window = compose_maps(window, (part[0], part[1]))
    length = first
    while length < count:
        parts = [from_behind(jnp.stack(window), by * length) for by in range(1, SCAN_RADIX) if by * length < count]
        joined = (parts[-1][0], parts[-1][1])
        for part in reversed(parts[:-1]):
            joined = compose_maps(joined, (part[0], part[1]))
        window = compose_maps(joined, window)
        length = length * (len(parts) + 1)
    return window[1], (carried[0] if extra else None)


def on_device(start_states, region_map, source, front):
    field_now = start_states[0]
    rows, cols = field_now.shape
    width = FINE
    slices = lax.axis_size("tm")
    slice_index = lax.axis_index("tm")
    scale = 2.0 * math.pi / (slices * FINE)

    stacked = jnp.stack(
        [field_now, region_map.astype(jnp.float32) + 1.0, source[0], source[1]], 0
    )
    extended = with_halo(stacked, width)
    code = extended[1]
    reluct = lookup_shifted(code, RELUCTIVITY)
    satur = lookup_shifted(code, SATURATION)
    mobile_ext = lookup_shifted(code, MOBILITY)
    src_cos, src_sin = extended[2], extended[3]
    row_rel = face_terms(reluct, 0)
    row_sat = face_terms(satur, 0)
    col_rel = face_terms(reluct, 1)
    col_sat = face_terms(satur, 1)
    mobile = mobile_ext[width : width + rows]

    def single_step(values, step_index):
        divergence, diagonal = flux_terms(values, row_rel, row_sat, col_rel, col_sat)
        phase_angle = (slice_index * FINE + step_index).astype(jnp.float32) * scale
        current = src_cos * jnp.cos(phase_angle) + src_sin * jnp.sin(phase_angle)
        return values + mobile_ext * (divergence + current), diagonal

    cut_slice = (front - 1) % slices
    keep_map = slice_index != cut_slice
    values_ext = extended[0]
    for sweep in range(ITERS):
        if sweep > 0:
            values_ext = with_halo(field_now, width)
        fine_values, fine_diagonal = single_step(values_ext, 0)
        for step_index in range(1, FINE):
            fine_values = single_step(fine_values, step_index)[0]
        fine_end = fine_values[width : width + rows]
        diagonal = fine_diagonal[width : width + rows]
        decay = 1.0 / (1.0 + FINE * mobile * diagonal)
        decay = jnp.where(keep_map, decay, 0.0)
        offset = fine_end - decay * field_now
        last = sweep == ITERS - 1
        field_now, previous_end = periodic_states(decay, offset, [fine_end] if last else [])
    jumps = previous_end[0] - field_now
    return (field_now[None], jumps[None])


def solution(mesh):
    placed = (P("tm", "space", None), P("space", None), P(None, "space", None), P())
    return jax.shard_map(
        on_device,
        mesh=mesh,
        in_specs=placed,
        out_specs=(P("tm", "space", None), P("tm", "space", None)),
        check_vma=False,
    )
```

```python
import math

import jax
import jax.numpy as jnp
from jax import lax
from jax.sharding import PartitionSpec as P

FINE = 16
ITERS = 2
SCAN_RADIX = 4


RELUCTIVITY = (1.0, 0.3, 1.0, 0.25)
SATURATION = (0.0, 2.0, 0.0, 1.5)
MOBILITY = (0.15, 0.02, 0.0004, 0.0008)


def with_halo(block, width):
    count = lax.axis_size("space")
    rows = block.shape[-2]
    forward = [(i, i + 1) for i in range(count - 1)]
    backward = [(i + 1, i) for i in range(count - 1)]
    above = lax.ppermute(lax.slice_in_dim(block, rows - width, rows, axis=block.ndim - 2), "space", forward)
    below = lax.ppermute(lax.slice_in_dim(block, 0, width, axis=block.ndim - 2), "space", backward)
    return jnp.concatenate([above, block, below], axis=block.ndim - 2)


def lookup_shifted(code, table):
    result = jnp.zeros(code.shape, jnp.float32)
    for region, entry_value in enumerate(table):
        result = result + jnp.where(code == jnp.float32(region + 1), jnp.float32(entry_value), jnp.float32(0.0))
    return result


def face_terms(values, axis):
    pad = [(0, 0)] * values.ndim
    pad[axis] = (1, 1)
    padded = jnp.pad(values, pad)
    n = padded.shape[axis]
    return 0.5 * (lax.slice_in_dim(padded, 0, n - 1, axis=axis) + lax.slice_in_dim(padded, 1, n, axis=axis))


def flux_terms(field, row_rel, row_sat, col_rel, col_sat):
    rows, cols = field.shape
    rpad = jnp.pad(field, ((1, 1), (0, 0)))
    row_diff = rpad[1:] - rpad[:-1]
    row_sq = row_diff * row_diff
    row_w = row_rel * (1.0 + row_sat * row_sq / (1.0 + row_sq))
    row_flux = row_w * row_diff
    cpad = jnp.pad(field, ((0, 0), (1, 1)))
    col_diff = cpad[:, 1:] - cpad[:, :-1]
    col_sq = col_diff * col_diff
    col_w = col_rel * (1.0 + col_sat * col_sq / (1.0 + col_sq))
    col_flux = col_w * col_diff
    divergence = (((-row_flux[:-1]) + row_flux[1:]) + (-col_flux[:, :-1])) + col_flux[:, 1:]
    diagonal = ((row_w[:-1] + row_w[1:]) + col_w[:, :-1]) + col_w[:, 1:]
    return divergence, diagonal


def compose_maps(earlier, later):
    return (later[0] * earlier[0], later[0] * earlier[1] + later[1])


def periodic_states(decay, offset, extra):
    count = lax.axis_size("tm")

    def from_behind(x, by):
        return lax.ppermute(x, "tm", [(i, (i + by) % count) for i in range(count)])

    own = jnp.stack([decay, offset])
    first = min(SCAN_RADIX, count)
    got = [from_behind(jnp.stack([decay, offset] + extra), 1)]
    got += [from_behind(own, by) for by in range(2, first + 1)]
    carried = [part[2:] for part in got[:1]]
    window = (got[-1][0], got[-1][1])
    for part in reversed(got[:-1]):
        window = compose_maps(window, (part[0], part[1]))
    length = first
    while length < count:
        parts = [from_behind(jnp.stack(window), by * length) for by in range(1, SCAN_RADIX) if by * length < count]
        joined = (parts[-1][0], parts[-1][1])
        for part in reversed(parts[:-1]):
            joined = compose_maps(joined, (part[0], part[1]))
        window = compose_maps(joined, window)
        length = length * (len(parts) + 1)
    return window[1], (carried[0] if extra else None)


def shift_down(x, by, fill):
    head = jnp.full(x.shape[:1] + (by,) + x.shape[2:], fill, x.dtype)
    return jnp.concatenate([head, x[:, : x.shape[1] - by]], axis=1)


def transposed_states(decay, offset, extra):
    count = lax.axis_size("tm")
    rows, cols = decay.shape
    parts = jnp.stack([decay, offset] + extra).reshape(2 + len(extra), count, rows * cols // count)
    cells = lax.all_to_all(parts, "tm", 1, 1, tiled=True)
    factor, shift = cells[0], cells[1]
    span = 1
    while span < count:
        earlier_factor = shift_down(factor[None], span, 1.0)[0]
        earlier_shift = shift_down(shift[None], span, 0.0)[0]
        factor, shift = factor * earlier_factor, factor * earlier_shift + shift
        span *= 2
    closing = shift[count - 1 :]
    before_factor = shift_down(factor[None], 1, 1.0)[0]
    before_shift = shift_down(shift[None], 1, 0.0)[0]
    states = before_factor * closing + before_shift
    outs = [states]
    if extra:
        ends = cells[2]
        outs.append(jnp.concatenate([ends[count - 1 :], ends[: count - 1]], axis=0) - states)
    back = lax.all_to_all(jnp.stack(outs), "tm", 1, 1, tiled=True)
    back = back.reshape(len(outs), rows, cols)
    return back[0], (back[1:] if extra else None)


def on_device(start_states, region_map, source, front):
    field_now = start_states[0]
    rows, cols = field_now.shape
    width = FINE
    slices = lax.axis_size("tm")
    slice_index = lax.axis_index("tm")
    scale = 2.0 * math.pi / (slices * FINE)

    stacked = jnp.stack(
        [field_now, region_map.astype(jnp.float32) + 1.0, source[0], source[1]], 0
    )
    extended = with_halo(stacked, width)
    code = extended[1]
    reluct = lookup_shifted(code, RELUCTIVITY)
    satur = lookup_shifted(code, SATURATION)
    mobile_ext = lookup_shifted(code, MOBILITY)
    src_cos, src_sin = extended[2], extended[3]
    row_rel = face_terms(reluct, 0)
    row_sat = face_terms(satur, 0)
    col_rel = face_terms(reluct, 1)
    col_sat = face_terms(satur, 1)
    mobile = mobile_ext[width : width + rows]

    def single_step(values, step_index):
        divergence, diagonal = flux_terms(values, row_rel, row_sat, col_rel, col_sat)
        phase_angle = (slice_index * FINE + step_index).astype(jnp.float32) * scale
        current = src_cos * jnp.cos(phase_angle) + src_sin * jnp.sin(phase_angle)
        return values + mobile_ext * (divergence + current), diagonal

    cut_slice = (front - 1) % slices
    keep_map = slice_index != cut_slice
    values_ext = extended[0]
    for sweep in range(ITERS):
        if sweep > 0:
            values_ext = with_halo(field_now, width)
        fine_values, fine_diagonal = single_step(values_ext, 0)
        for step_index in range(1, FINE):
            fine_values = single_step(fine_values, step_index)[0]
        fine_end = fine_values[width : width + rows]
        diagonal = fine_diagonal[width : width + rows]
        decay = 1.0 / (1.0 + FINE * mobile * diagonal)
        decay = jnp.where(keep_map, decay, 0.0)
        offset = fine_end - decay * field_now
        last = sweep == ITERS - 1
        field_now, jumps = transposed_states(decay, offset, [fine_end] if last else [])
    return (field_now[None], jumps)


def solution(mesh):
    placed = (P("tm", "space", None), P("space", None), P(None, "space", None), P())
    return jax.shard_map(
        on_device,
        mesh=mesh,
        in_specs=placed,
        out_specs=(P("tm", "space", None), P("tm", "space", None)),
        check_vma=False,
    )
```

```python
import math

import jax
import jax.numpy as jnp
from jax import lax
from jax.sharding import PartitionSpec as P

FINE = 16
ITERS = 2
SCAN_RADIX = 4


RELUCTIVITY = (1.0, 0.3, 1.0, 0.25)
SATURATION = (0.0, 2.0, 0.0, 1.5)
MOBILITY = (0.15, 0.02, 0.0004, 0.0008)


def with_halo(block, width):
    count = lax.axis_size("space")
    rows = block.shape[-2]
    forward = [(i, i + 1) for i in range(count - 1)]
    backward = [(i + 1, i) for i in range(count - 1)]
    above = lax.ppermute(lax.slice_in_dim(block, rows - width, rows, axis=block.ndim - 2), "space", forward)
    below = lax.ppermute(lax.slice_in_dim(block, 0, width, axis=block.ndim - 2), "space", backward)
    return jnp.concatenate([above, block, below], axis=block.ndim - 2)


def lookup_shifted(code, table):
    result = jnp.zeros(code.shape, jnp.float32)
    for region, entry_value in enumerate(table):
        result = result + jnp.where(code == jnp.float32(region + 1), jnp.float32(entry_value), jnp.float32(0.0))
    return result


def face_terms(values, axis):
    pad = [(0, 0)] * values.ndim
    pad[axis] = (1, 1)
    padded = jnp.pad(values, pad)
    n = padded.shape[axis]
    return 0.5 * (lax.slice_in_dim(padded, 0, n - 1, axis=axis) + lax.slice_in_dim(padded, 1, n, axis=axis))


def flux_terms(field, row_rel, row_sat, col_rel, col_sat):
    rows, cols = field.shape
    rpad = jnp.pad(field, ((1, 1), (0, 0)))
    row_diff = rpad[1:] - rpad[:-1]
    row_sq = row_diff * row_diff
    row_w = row_rel * (1.0 + row_sat * row_sq / (1.0 + row_sq))
    row_flux = row_w * row_diff
    cpad = jnp.pad(field, ((0, 0), (1, 1)))
    col_diff = cpad[:, 1:] - cpad[:, :-1]
    col_sq = col_diff * col_diff
    col_w = col_rel * (1.0 + col_sat * col_sq / (1.0 + col_sq))
    col_flux = col_w * col_diff
    divergence = (((-row_flux[:-1]) + row_flux[1:]) + (-col_flux[:, :-1])) + col_flux[:, 1:]
    diagonal = ((row_w[:-1] + row_w[1:]) + col_w[:, :-1]) + col_w[:, 1:]
    return divergence, diagonal


def compose_maps(earlier, later):
    return (later[0] * earlier[0], later[0] * earlier[1] + later[1])


def periodic_states(decay, offset, extra):
    count = lax.axis_size("tm")

    def from_behind(x, by):
        return lax.ppermute(x, "tm", [(i, (i + by) % count) for i in range(count)])

    own = jnp.stack([decay, offset])
    first = min(SCAN_RADIX, count)
    got = [from_behind(jnp.stack([decay, offset] + extra), 1)]
    got += [from_behind(own, by) for by in range(2, first + 1)]
    carried = [part[2:] for part in got[:1]]
    window = (got[-1][0], got[-1][1])
    for part in reversed(got[:-1]):
        window = compose_maps(window, (part[0], part[1]))
    length = first
    while length < count:
        parts = [from_behind(jnp.stack(window), by * length) for by in range(1, SCAN_RADIX) if by * length < count]
        joined = (parts[-1][0], parts[-1][1])
        for part in reversed(parts[:-1]):
            joined = compose_maps(joined, (part[0], part[1]))
        window = compose_maps(joined, window)
        length = length * (len(parts) + 1)
    return window[1], (carried[0] if extra else None)


def shift_down(x, by, fill):
    head = jnp.full(x.shape[:1] + (by,) + x.shape[2:], fill, x.dtype)
    return jnp.concatenate([head, x[:, : x.shape[1] - by]], axis=1)


def transposed_states(decay, offset, extra):
    count = lax.axis_size("tm")
    rows, cols = decay.shape
    parts = jnp.stack([decay, offset] + extra).reshape(2 + len(extra), count, rows * cols // count)
    cells = lax.all_to_all(parts, "tm", 1, 1, tiled=True)
    factor, shift = cells[0], cells[1]
    span = 1
    while span < count:
        earlier_factor = shift_down(factor[None], span, 1.0)[0]
        earlier_shift = shift_down(shift[None], span, 0.0)[0]
        factor, shift = factor * earlier_factor, factor * earlier_shift + shift
        span *= 2
    closing = shift[count - 1 :]
    before_factor = shift_down(factor[None], 1, 1.0)[0]
    before_shift = shift_down(shift[None], 1, 0.0)[0]
    states = before_factor * closing + before_shift
    outs = [states]
    if extra:
        ends = cells[2]
        outs.append(jnp.concatenate([ends[count - 1 :], ends[: count - 1]], axis=0) - states)
    back = lax.all_to_all(jnp.stack(outs), "tm", 1, 1, tiled=True)
    back = back.reshape(len(outs), rows, cols)
    return back[0], (back[1:] if extra else None)


def on_device(start_states, region_map, source, front):
    field_now = start_states[0]
    rows, cols = field_now.shape
    width = FINE
    reach = ITERS * FINE if ITERS * FINE <= rows else FINE
    slices = lax.axis_size("tm")
    slice_index = lax.axis_index("tm")
    scale = 2.0 * math.pi / (slices * FINE)

    stacked = jnp.stack(
        [field_now, region_map.astype(jnp.float32) + 1.0, source[0], source[1]], 0
    )
    extended = with_halo(stacked, reach)
    code = extended[1]
    reluct = lookup_shifted(code, RELUCTIVITY)
    satur = lookup_shifted(code, SATURATION)
    mobile_all = lookup_shifted(code, MOBILITY)
    cos_all, sin_all = extended[2], extended[3]
    cut_slice = (front - 1) % slices
    keep_map = slice_index != cut_slice

    def fine_solve(values, low, high):
        row_rel = face_terms(reluct[low:high], 0)
        row_sat = face_terms(satur[low:high], 0)
        col_rel = face_terms(reluct[low:high], 1)
        col_sat = face_terms(satur[low:high], 1)
        mobile_ext = mobile_all[low:high]
        src_cos, src_sin = cos_all[low:high], sin_all[low:high]

        def single_step(values, step_index):
            divergence, diagonal = flux_terms(values, row_rel, row_sat, col_rel, col_sat)
            phase_angle = (slice_index * FINE + step_index).astype(jnp.float32) * scale
            current = src_cos * jnp.cos(phase_angle) + src_sin * jnp.sin(phase_angle)
            return values + mobile_ext * (divergence + current), diagonal

        fine_values, fine_diagonal = single_step(values, 0)
        for step_index in range(1, FINE):
            fine_values = single_step(fine_values, step_index)[0]
        return fine_values, fine_diagonal

    values_ext = extended[0]
    low, high = 0, rows + 2 * reach
    for sweep in range(ITERS):
        last = sweep == ITERS - 1
        if low == high:
            values_ext = with_halo(field_now, width)
            low, high = reach - width, reach + rows + width
        fine_values, fine_diagonal = fine_solve(values_ext, low, high)
        keep_low, keep_high = FINE, high - low - FINE
        fine_end = fine_values[keep_low:keep_high]
        diagonal = fine_diagonal[keep_low:keep_high]
        start_now = values_ext[keep_low:keep_high]
        mobile = mobile_all[low + keep_low : low + keep_high]
        decay = 1.0 / (1.0 + FINE * mobile * diagonal)
        decay = jnp.where(keep_map, decay, 0.0)
        offset = fine_end - decay * start_now
        field_now, jumps = transposed_states(decay, offset, [fine_end] if last else [])
        values_ext = field_now
        low, high = low + keep_low, low + keep_high
        if high - low == rows:
            low = high
    return (field_now[None], jumps)


def solution(mesh):
    placed = (P("tm", "space", None), P("space", None), P(None, "space", None), P())
    return jax.shard_map(
        on_device,
        mesh=mesh,
        in_specs=placed,
        out_specs=(P("tm", "space", None), P("tm", "space", None)),
        check_vma=False,
    )
```

```python
import math

import jax
import jax.numpy as jnp
from jax import lax
from jax.sharding import PartitionSpec as P

FINE = 16
ITERS = 2
SCAN_RADIX = 4


RELUCTIVITY = (1.0, 0.3, 1.0, 0.25)
SATURATION = (0.0, 2.0, 0.0, 1.5)
MOBILITY = (0.15, 0.02, 0.0004, 0.0008)


def with_halo(block, width):
    count = lax.axis_size("space")
    rows = block.shape[-2]
    forward = [(i, i + 1) for i in range(count - 1)]
    backward = [(i + 1, i) for i in range(count - 1)]
    above = lax.ppermute(lax.slice_in_dim(block, rows - width, rows, axis=block.ndim - 2), "space", forward)
    below = lax.ppermute(lax.slice_in_dim(block, 0, width, axis=block.ndim - 2), "space", backward)
    return jnp.concatenate([above, block, below], axis=block.ndim - 2)


def lookup_shifted(code, table):
    result = jnp.zeros(code.shape, jnp.float32)
    for region, entry_value in enumerate(table):
        result = result + jnp.where(code == jnp.float32(region + 1), jnp.float32(entry_value), jnp.float32(0.0))
    return result


def face_terms(values, axis):
    pad = [(0, 0)] * values.ndim
    pad[axis] = (1, 1)
    padded = jnp.pad(values, pad)
    n = padded.shape[axis]
    return 0.5 * (lax.slice_in_dim(padded, 0, n - 1, axis=axis) + lax.slice_in_dim(padded, 1, n, axis=axis))


def flux_terms(field, row_rel, row_sat, col_rel, col_sat):
    rows, cols = field.shape
    rpad = jnp.pad(field, ((1, 1), (0, 0)))
    row_diff = rpad[1:] - rpad[:-1]
    row_sq = row_diff * row_diff
    row_w = row_rel * (1.0 + row_sat * row_sq / (1.0 + row_sq))
    row_flux = row_w * row_diff
    cpad = jnp.pad(field, ((0, 0), (1, 1)))
    col_diff = cpad[:, 1:] - cpad[:, :-1]
    col_sq = col_diff * col_diff
    col_w = col_rel * (1.0 + col_sat * col_sq / (1.0 + col_sq))
    col_flux = col_w * col_diff
    divergence = (((-row_flux[:-1]) + row_flux[1:]) + (-col_flux[:, :-1])) + col_flux[:, 1:]
    diagonal = ((row_w[:-1] + row_w[1:]) + col_w[:, :-1]) + col_w[:, 1:]
    return divergence, diagonal


def compose_maps(earlier, later):
    return (later[0] * earlier[0], later[0] * earlier[1] + later[1])


def periodic_states(decay, offset, extra):
    count = lax.axis_size("tm")

    def from_behind(x, by):
        return lax.ppermute(x, "tm", [(i, (i + by) % count) for i in range(count)])

    own = jnp.stack([decay, offset])
    first = min(SCAN_RADIX, count)
    got = [from_behind(jnp.stack([decay, offset] + extra), 1)]
    got += [from_behind(own, by) for by in range(2, first + 1)]
    carried = [part[2:] for part in got[:1]]
    window = (got[-1][0], got[-1][1])
    for part in reversed(got[:-1]):
        window = compose_maps(window, (part[0], part[1]))
    length = first
    while length < count:
        parts = [from_behind(jnp.stack(window), by * length) for by in range(1, SCAN_RADIX) if by * length < count]
        joined = (parts[-1][0], parts[-1][1])
        for part in reversed(parts[:-1]):
            joined = compose_maps(joined, (part[0], part[1]))
        window = compose_maps(joined, window)
        length = length * (len(parts) + 1)
    return window[1], (carried[0] if extra else None)


def shift_down(x, by, fill):
    head = jnp.full(x.shape[:1] + (by,) + x.shape[2:], fill, x.dtype)
    return jnp.concatenate([head, x[:, : x.shape[1] - by]], axis=1)


def transposed_states(decay, offset, extra):
    count = lax.axis_size("tm")
    rows, cols = decay.shape
    parts = jnp.stack([decay, offset] + extra).reshape(2 + len(extra), count, rows * cols // count)
    cells = lax.all_to_all(parts, "tm", 1, 1, tiled=True)
    factor, shift = cells[0], cells[1]
    span = 1
    while span < count:
        earlier_factor = shift_down(factor[None], span, 1.0)[0]
        earlier_shift = shift_down(shift[None], span, 0.0)[0]
        factor, shift = factor * earlier_factor, factor * earlier_shift + shift
        span *= 2
    closing = shift[count - 1 :]
    before_factor = shift_down(factor[None], 1, 1.0)[0]
    before_shift = shift_down(shift[None], 1, 0.0)[0]
    states = before_factor * closing + before_shift
    outs = [states]
    if extra:
        ends = cells[2]
        outs.append(jnp.concatenate([ends[count - 1 :], ends[: count - 1]], axis=0) - states)
    back = lax.all_to_all(jnp.stack(outs), "tm", 1, 1, tiled=True)
    back = back.reshape(len(outs), rows, cols)
    return back[0], (back[1:] if extra else None)


def scan_over_time(factor, shift):
    count = factor.shape[0]
    span = 1
    while span < count:
        earlier_factor = shift_down(factor[None], span, 1.0)[0]
        earlier_shift = shift_down(shift[None], span, 0.0)[0]
        factor, shift = factor * earlier_factor, factor * earlier_shift + shift
        span *= 2
    closing = shift[count - 1 :]
    before_factor = shift_down(factor[None], 1, 1.0)[0]
    before_shift = shift_down(shift[None], 1, 0.0)[0]
    return before_factor * closing + before_shift


def exchange(parts):
    return lax.all_to_all(parts, "tm", 1, 1, tiled=True)


def on_device(start_states, region_map, source, front):
    field_now = start_states[0]
    rows, cols = field_now.shape
    width = FINE
    slices = lax.axis_size("tm")
    reach = 2 * FINE
    assert ITERS == 2 and reach <= rows and (rows * cols) % slices == 0 and (2 * width * cols) % slices == 0
    slice_index = lax.axis_index("tm")
    scale = 2.0 * math.pi / (slices * FINE)

    stacked = jnp.stack(
        [field_now, region_map.astype(jnp.float32) + 1.0, source[0], source[1]], 0
    )
    extended = with_halo(stacked, reach)
    code = extended[1]
    reluct = lookup_shifted(code, RELUCTIVITY)
    satur = lookup_shifted(code, SATURATION)
    mobile_all = lookup_shifted(code, MOBILITY)
    cos_all, sin_all = extended[2], extended[3]
    cut_slice = (front - 1) % slices
    keep_map = slice_index != cut_slice

    def fine_solve(values, low, high):
        row_rel = face_terms(reluct[low:high], 0)
        row_sat = face_terms(satur[low:high], 0)
        col_rel = face_terms(reluct[low:high], 1)
        col_sat = face_terms(satur[low:high], 1)
        mobile_ext = mobile_all[low:high]
        src_cos, src_sin = cos_all[low:high], sin_all[low:high]

        def single_step(values, step_index):
            divergence, diagonal = flux_terms(values, row_rel, row_sat, col_rel, col_sat)
            phase_angle = (slice_index * FINE + step_index).astype(jnp.float32) * scale
            current = src_cos * jnp.cos(phase_angle) + src_sin * jnp.sin(phase_angle)
            return values + mobile_ext * (divergence + current), diagonal

        fine_values, fine_diagonal = single_step(values, 0)
        for step_index in range(1, FINE):
            fine_values = single_step(fine_values, step_index)[0]
        fine_values = fine_values[FINE : high - low - FINE]
        fine_diagonal = fine_diagonal[FINE : high - low - FINE]
        mobile = mobile_all[low + FINE : high - FINE]
        decay = 1.0 / (1.0 + FINE * mobile * fine_diagonal)
        return fine_values, jnp.where(keep_map, decay, 0.0)

    own_cells = rows * cols // slices

    def to_chunks(block):
        own = block[width : width + rows].reshape(slices, own_cells)
        halo = jnp.concatenate([block[:width], block[width + rows :]], 0).reshape(slices, -1)
        return jnp.concatenate([own, halo], 1)

    def from_chunks(chunks):
        own = chunks[:, :own_cells].reshape(rows, cols)
        halo = chunks[:, own_cells:].reshape(2 * width, cols)
        return jnp.concatenate([halo[:width], own, halo[width:]], 0)

    fine_end, decay = fine_solve(extended[0], 0, rows + 2 * reach)
    offset = fine_end - decay * extended[0][width : width + rows + 2 * width]
    timed = exchange(jnp.stack([to_chunks(decay), to_chunks(offset)]))
    states_timed = scan_over_time(timed[0], timed[1])
    strip_timed = states_timed[:, :own_cells]
    field_block = from_chunks(exchange(states_timed[None])[0])

    fine_end, decay = fine_solve(field_block, width, rows + 3 * width)
    timed = exchange(jnp.stack([decay.reshape(slices, own_cells), fine_end.reshape(slices, own_cells)]))
    offset_timed = timed[1] - timed[0] * strip_timed
    states_timed = scan_over_time(timed[0], offset_timed)
    ends_timed = timed[1]
    jumps_timed = jnp.concatenate([ends_timed[slices - 1 :], ends_timed[: slices - 1]], 0) - states_timed
    back = exchange(jnp.stack([states_timed, jumps_timed])).reshape(2, 1, rows, cols)
    return (back[0], back[1])


def solution(mesh):
    placed = (P("tm", "space", None), P("space", None), P(None, "space", None), P())
    return jax.shard_map(
        on_device,
        mesh=mesh,
        in_specs=placed,
        out_specs=(P("tm", "space", None), P("tm", "space", None)),
        check_vma=False,
    )
```

```python
import math

import jax
import jax.numpy as jnp
from jax import lax
from jax.sharding import PartitionSpec as P

FINE = 16
ITERS = 2
SCAN_RADIX = 4


RELUCTIVITY = (1.0, 0.3, 1.0, 0.25)
SATURATION = (0.0, 2.0, 0.0, 1.5)
MOBILITY = (0.15, 0.02, 0.0004, 0.0008)


def with_halo(block, width):
    count = lax.axis_size("space")
    rows = block.shape[-2]
    forward = [(i, i + 1) for i in range(count - 1)]
    backward = [(i + 1, i) for i in range(count - 1)]
    above = lax.ppermute(lax.slice_in_dim(block, rows - width, rows, axis=block.ndim - 2), "space", forward)
    below = lax.ppermute(lax.slice_in_dim(block, 0, width, axis=block.ndim - 2), "space", backward)
    return jnp.concatenate([above, block, below], axis=block.ndim - 2)


def lookup_shifted(code, table):
    result = jnp.zeros(code.shape, jnp.float32)
    for region, entry_value in enumerate(table):
        result = result + jnp.where(code == jnp.float32(region + 1), jnp.float32(entry_value), jnp.float32(0.0))
    return result


def face_terms(values, axis):
    pad = [(0, 0)] * values.ndim
    pad[axis] = (1, 1)
    padded = jnp.pad(values, pad)
    n = padded.shape[axis]
    return 0.5 * (lax.slice_in_dim(padded, 0, n - 1, axis=axis) + lax.slice_in_dim(padded, 1, n, axis=axis))


def flux_terms(field, row_rel, row_sat, col_rel, col_sat):
    rows, cols = field.shape
    rpad = jnp.pad(field, ((1, 1), (0, 0)))
    row_diff = rpad[1:] - rpad[:-1]
    row_sq = row_diff * row_diff
    row_w = row_rel * (1.0 + row_sat * row_sq / (1.0 + row_sq))
    row_flux = row_w * row_diff
    cpad = jnp.pad(field, ((0, 0), (1, 1)))
    col_diff = cpad[:, 1:] - cpad[:, :-1]
    col_sq = col_diff * col_diff
    col_w = col_rel * (1.0 + col_sat * col_sq / (1.0 + col_sq))
    col_flux = col_w * col_diff
    divergence = (((-row_flux[:-1]) + row_flux[1:]) + (-col_flux[:, :-1])) + col_flux[:, 1:]
    diagonal = ((row_w[:-1] + row_w[1:]) + col_w[:, :-1]) + col_w[:, 1:]
    return divergence, diagonal


def compose_maps(earlier, later):
    return (later[0] * earlier[0], later[0] * earlier[1] + later[1])


def periodic_states(decay, offset, extra):
    count = lax.axis_size("tm")

    def from_behind(x, by):
        return lax.ppermute(x, "tm", [(i, (i + by) % count) for i in range(count)])

    own = jnp.stack([decay, offset])
    first = min(SCAN_RADIX, count)
    got = [from_behind(jnp.stack([decay, offset] + extra), 1)]
    got += [from_behind(own, by) for by in range(2, first + 1)]
    carried = [part[2:] for part in got[:1]]
    window = (got[-1][0], got[-1][1])
    for part in reversed(got[:-1]):
        window = compose_maps(window, (part[0], part[1]))
    length = first
    while length < count:
        parts = [from_behind(jnp.stack(window), by * length) for by in range(1, SCAN_RADIX) if by * length < count]
        joined = (parts[-1][0], parts[-1][1])
        for part in reversed(parts[:-1]):
            joined = compose_maps(joined, (part[0], part[1]))
        window = compose_maps(joined, window)
        length = length * (len(parts) + 1)
    return window[1], (carried[0] if extra else None)


def shift_down(x, by, fill):
    head = jnp.full(x.shape[:1] + (by,) + x.shape[2:], fill, x.dtype)
    return jnp.concatenate([head, x[:, : x.shape[1] - by]], axis=1)


def transposed_states(decay, offset, extra):
    count = lax.axis_size("tm")
    rows, cols = decay.shape
    parts = jnp.stack([decay, offset] + extra).reshape(2 + len(extra), count, rows * cols // count)
    cells = lax.all_to_all(parts, "tm", 1, 1, tiled=True)
    factor, shift = cells[0], cells[1]
    span = 1
    while span < count:
        earlier_factor = shift_down(factor[None], span, 1.0)[0]
        earlier_shift = shift_down(shift[None], span, 0.0)[0]
        factor, shift = factor * earlier_factor, factor * earlier_shift + shift
        span *= 2
    closing = shift[count - 1 :]
    before_factor = shift_down(factor[None], 1, 1.0)[0]
    before_shift = shift_down(shift[None], 1, 0.0)[0]
    states = before_factor * closing + before_shift
    outs = [states]
    if extra:
        ends = cells[2]
        outs.append(jnp.concatenate([ends[count - 1 :], ends[: count - 1]], axis=0) - states)
    back = lax.all_to_all(jnp.stack(outs), "tm", 1, 1, tiled=True)
    back = back.reshape(len(outs), rows, cols)
    return back[0], (back[1:] if extra else None)


def scan_over_time(factor, shift):
    count = factor.shape[0]
    span = 1
    while span < count:
        earlier_factor = shift_down(factor[None], span, 1.0)[0]
        earlier_shift = shift_down(shift[None], span, 0.0)[0]
        factor, shift = factor * earlier_factor, factor * earlier_shift + shift
        span *= 2
    closing = shift[count - 1 :]
    before_factor = shift_down(factor[None], 1, 1.0)[0]
    before_shift = shift_down(shift[None], 1, 0.0)[0]
    return before_factor * closing + before_shift


def exchange(parts):
    return lax.all_to_all(parts, "tm", 1, 1, tiled=True)


def on_device(start_states, region_map, source, front):
    field_now = start_states[0]
    rows, cols = field_now.shape
    width = FINE
    slices = lax.axis_size("tm")
    reach = 2 * FINE
    assert ITERS == 2 and reach <= rows and (rows * cols) % slices == 0 and (2 * width * cols) % slices == 0
    slice_index = lax.axis_index("tm")
    scale = 2.0 * math.pi / (slices * FINE)

    stacked = jnp.stack(
        [field_now, region_map.astype(jnp.float32) + 1.0, source[0], source[1]], 0
    )
    extended = with_halo(stacked, reach)
    code = extended[1]
    reluct = lookup_shifted(code, RELUCTIVITY)
    satur = lookup_shifted(code, SATURATION)
    mobile_all = lookup_shifted(code, MOBILITY)
    cos_all, sin_all = extended[2], extended[3]
    cut_slice = (front - 1) % slices
    keep_map = slice_index != cut_slice

    def single_step(values, step_index, low, high):
        row_rel = face_terms(reluct[low:high], 0)
        row_sat = face_terms(satur[low:high], 0)
        col_rel = face_terms(reluct[low:high], 1)
        col_sat = face_terms(satur[low:high], 1)
        divergence, diagonal = flux_terms(values, row_rel, row_sat, col_rel, col_sat)
        phase_angle = (slice_index * FINE + step_index).astype(jnp.float32) * scale
        current = cos_all[low:high] * jnp.cos(phase_angle) + sin_all[low:high] * jnp.sin(phase_angle)
        return values + mobile_all[low:high] * (divergence + current), diagonal

    def fine_solve(values, low, high):
        fine_values, fine_diagonal = single_step(values, 0, low, high)
        trim = 0
        for step_index in range(1, FINE):
            if step_index >= trim + 8:
                trim += 8
                fine_values = fine_values[8:-8]
            fine_values = single_step(fine_values, step_index, low + trim, high - trim)[0]
        fine_values = fine_values[FINE - trim : high - low - FINE - trim]
        fine_diagonal = fine_diagonal[FINE : high - low - FINE]
        mobile = mobile_all[low + FINE : high - FINE]
        decay = 1.0 / (1.0 + FINE * mobile * fine_diagonal)
        return fine_values, jnp.where(keep_map, decay, 0.0)

    own_cells = rows * cols // slices

    def to_chunks(block):
        own = block[width : width + rows].reshape(slices, own_cells)
        halo = jnp.concatenate([block[:width], block[width + rows :]], 0).reshape(slices, -1)
        return jnp.concatenate([own, halo], 1)

    def from_chunks(chunks):
        own = chunks[:, :own_cells].reshape(rows, cols)
        halo = chunks[:, own_cells:].reshape(2 * width, cols)
        return jnp.concatenate([halo[:width], own, halo[width:]], 0)

    fine_end, decay = fine_solve(extended[0], 0, rows + 2 * reach)
    offset = fine_end - decay * extended[0][width : width + rows + 2 * width]
    timed = exchange(jnp.stack([to_chunks(decay), to_chunks(offset)]))
    states_timed = scan_over_time(timed[0], timed[1])
    strip_timed = states_timed[:, :own_cells]
    field_block = from_chunks(lax.all_to_all(states_timed, "tm", 0, 0, tiled=True))

    fine_end, decay = fine_solve(field_block, width, rows + 3 * width)
    timed = exchange(jnp.stack([decay.reshape(slices, own_cells), fine_end.reshape(slices, own_cells)]))
    offset_timed = timed[1] - timed[0] * strip_timed
    states_timed = scan_over_time(timed[0], offset_timed)
    ends_timed = timed[1]
    jumps_timed = jnp.concatenate([ends_timed[slices - 1 :], ends_timed[: slices - 1]], 0) - states_timed
    back = exchange(jnp.stack([states_timed, jumps_timed])).reshape(2, 1, rows, cols)
    return (back[0], back[1])


def solution(mesh):
    placed = (P("tm", "space", None), P("space", None), P(None, "space", None), P())
    return jax.shard_map(
        on_device,
        mesh=mesh,
        in_specs=placed,
        out_specs=(P("tm", "space", None), P("tm", "space", None)),
        check_vma=False,
    )
```

```python
import math

import jax
import jax.numpy as jnp
from jax import lax
from jax.sharding import PartitionSpec as P

FINE = 16
ITERS = 2
SCAN_RADIX = 4


RELUCTIVITY = (1.0, 0.3, 1.0, 0.25)
SATURATION = (0.0, 2.0, 0.0, 1.5)
MOBILITY = (0.15, 0.02, 0.0004, 0.0008)


def with_halo(block, width):
    count = lax.axis_size("space")
    rows = block.shape[-2]
    forward = [(i, i + 1) for i in range(count - 1)]
    backward = [(i + 1, i) for i in range(count - 1)]
    above = lax.ppermute(lax.slice_in_dim(block, rows - width, rows, axis=block.ndim - 2), "space", forward)
    below = lax.ppermute(lax.slice_in_dim(block, 0, width, axis=block.ndim - 2), "space", backward)
    return jnp.concatenate([above, block, below], axis=block.ndim - 2)


def lookup_shifted(code, table):
    result = jnp.zeros(code.shape, jnp.float32)
    for region, entry_value in enumerate(table):
        result = result + jnp.where(code == jnp.float32(region + 1), jnp.float32(entry_value), jnp.float32(0.0))
    return result


def face_terms(values, axis):
    pad = [(0, 0)] * values.ndim
    pad[axis] = (1, 1)
    padded = jnp.pad(values, pad)
    n = padded.shape[axis]
    return 0.5 * (lax.slice_in_dim(padded, 0, n - 1, axis=axis) + lax.slice_in_dim(padded, 1, n, axis=axis))


def flux_terms(field, row_rel, row_sat, col_rel, col_sat):
    rows, cols = field.shape
    rpad = jnp.pad(field, ((1, 1), (0, 0)))
    row_diff = rpad[1:] - rpad[:-1]
    row_sq = row_diff * row_diff
    row_w = row_rel * (1.0 + row_sat * row_sq / (1.0 + row_sq))
    row_flux = row_w * row_diff
    cpad = jnp.pad(field, ((0, 0), (1, 1)))
    col_diff = cpad[:, 1:] - cpad[:, :-1]
    col_sq = col_diff * col_diff
    col_w = col_rel * (1.0 + col_sat * col_sq / (1.0 + col_sq))
    col_flux = col_w * col_diff
    divergence = (((-row_flux[:-1]) + row_flux[1:]) + (-col_flux[:, :-1])) + col_flux[:, 1:]
    diagonal = ((row_w[:-1] + row_w[1:]) + col_w[:, :-1]) + col_w[:, 1:]
    return divergence, diagonal


def compose_maps(earlier, later):
    return (later[0] * earlier[0], later[0] * earlier[1] + later[1])


def periodic_states(decay, offset, extra):
    count = lax.axis_size("tm")

    def from_behind(x, by):
        return lax.ppermute(x, "tm", [(i, (i + by) % count) for i in range(count)])

    own = jnp.stack([decay, offset])
    first = min(SCAN_RADIX, count)
    got = [from_behind(jnp.stack([decay, offset] + extra), 1)]
    got += [from_behind(own, by) for by in range(2, first + 1)]
    carried = [part[2:] for part in got[:1]]
    window = (got[-1][0], got[-1][1])
    for part in reversed(got[:-1]):
        window = compose_maps(window, (part[0], part[1]))
    length = first
    while length < count:
        parts = [from_behind(jnp.stack(window), by * length) for by in range(1, SCAN_RADIX) if by * length < count]
        joined = (parts[-1][0], parts[-1][1])
        for part in reversed(parts[:-1]):
            joined = compose_maps(joined, (part[0], part[1]))
        window = compose_maps(joined, window)
        length = length * (len(parts) + 1)
    return window[1], (carried[0] if extra else None)


def shift_down(x, by, fill):
    head = jnp.full(x.shape[:1] + (by,) + x.shape[2:], fill, x.dtype)
    return jnp.concatenate([head, x[:, : x.shape[1] - by]], axis=1)


def transposed_states(decay, offset, extra):
    count = lax.axis_size("tm")
    rows, cols = decay.shape
    parts = jnp.stack([decay, offset] + extra).reshape(2 + len(extra), count, rows * cols // count)
    cells = lax.all_to_all(parts, "tm", 1, 1, tiled=True)
    factor, shift = cells[0], cells[1]
    span = 1
    while span < count:
        earlier_factor = shift_down(factor[None], span, 1.0)[0]
        earlier_shift = shift_down(shift[None], span, 0.0)[0]
        factor, shift = factor * earlier_factor, factor * earlier_shift + shift
        span *= 2
    closing = shift[count - 1 :]
    before_factor = shift_down(factor[None], 1, 1.0)[0]
    before_shift = shift_down(shift[None], 1, 0.0)[0]
    states = before_factor * closing + before_shift
    outs = [states]
    if extra:
        ends = cells[2]
        outs.append(jnp.concatenate([ends[count - 1 :], ends[: count - 1]], axis=0) - states)
    back = lax.all_to_all(jnp.stack(outs), "tm", 1, 1, tiled=True)
    back = back.reshape(len(outs), rows, cols)
    return back[0], (back[1:] if extra else None)


def scan_over_time(factor, shift):
    count = factor.shape[0]
    span = 1
    while span < count:
        earlier_factor = shift_down(factor[None], span, 1.0)[0]
        earlier_shift = shift_down(shift[None], span, 0.0)[0]
        factor, shift = factor * earlier_factor, factor * earlier_shift + shift
        span *= 2
    closing = shift[count - 1 :]
    before_factor = shift_down(factor[None], 1, 1.0)[0]
    before_shift = shift_down(shift[None], 1, 0.0)[0]
    return before_factor * closing + before_shift


def exchange(parts):
    return lax.all_to_all(parts, "tm", 1, 1, tiled=True)


def on_device(start_states, region_map, source, front):
    field_now = start_states[0]
    rows, cols = field_now.shape
    width = FINE
    slices = lax.axis_size("tm")
    reach = 2 * FINE
    assert ITERS == 2 and reach <= rows and (rows * cols) % slices == 0 and (2 * width * cols) % slices == 0
    slice_index = lax.axis_index("tm")
    scale = 2.0 * math.pi / (slices * FINE)

    stacked = jnp.stack(
        [field_now, region_map.astype(jnp.float32) + 1.0, source[0], source[1]], 0
    )
    extended = with_halo(stacked, reach)
    code = extended[1]
    reluct = lookup_shifted(code, RELUCTIVITY)
    satur = lookup_shifted(code, SATURATION)
    mobile_all = lookup_shifted(code, MOBILITY)
    cos_all, sin_all = extended[2], extended[3]
    cut_slice = (front - 1) % slices
    keep_map = slice_index != cut_slice

    def fine_solve(values, low, high):
        row_rel = face_terms(reluct[low:high], 0)
        row_sat = face_terms(satur[low:high], 0)
        col_rel = face_terms(reluct[low:high], 1)
        col_sat = face_terms(satur[low:high], 1)
        mobile_ext = mobile_all[low:high]
        src_cos, src_sin = cos_all[low:high], sin_all[low:high]

        def single_step(values, step_index):
            divergence, diagonal = flux_terms(values, row_rel, row_sat, col_rel, col_sat)
            phase_angle = (slice_index * FINE + step_index).astype(jnp.float32) * scale
            current = src_cos * jnp.cos(phase_angle) + src_sin * jnp.sin(phase_angle)
            return values + mobile_ext * (divergence + current), diagonal

        fine_values, fine_diagonal = single_step(values, 0)
        for step_index in range(1, FINE):
            fine_values = single_step(fine_values, step_index)[0]
        fine_values = fine_values[FINE : high - low - FINE]
        fine_diagonal = fine_diagonal[FINE : high - low - FINE]
        mobile = mobile_all[low + FINE : high - FINE]
        decay = 1.0 / (1.0 + FINE * mobile * fine_diagonal)
        return fine_values, jnp.where(keep_map, decay, 0.0)

    own_cells = rows * cols // slices
    assert rows % 8 == 0 and cols % 128 == 0 and (2 * width) % 8 == 0

    def cells_of(x):
        n = x.shape[0]
        return x.reshape(n // 8, 8, cols // 128, 128).transpose(0, 2, 1, 3).reshape(slices, -1)

    def grid_of(chunks):
        n = chunks.size // cols
        return chunks.reshape(n // 8, cols // 128, 8, 128).transpose(0, 2, 1, 3).reshape(n, cols)

    def to_chunks(block):
        own = cells_of(block[width : width + rows])
        halo = cells_of(jnp.concatenate([block[:width], block[width + rows :]], 0))
        return jnp.concatenate([own, halo], 1)

    def from_chunks(chunks):
        own = grid_of(chunks[:, :own_cells])
        halo = grid_of(chunks[:, own_cells:])
        return jnp.concatenate([halo[:width], own, halo[width:]], 0)

    fine_end, decay = fine_solve(extended[0], 0, rows + 2 * reach)
    offset = fine_end - decay * extended[0][width : width + rows + 2 * width]
    timed = exchange(jnp.stack([to_chunks(decay), to_chunks(offset)]))
    states_timed = scan_over_time(timed[0], timed[1])
    strip_timed = states_timed[:, :own_cells]
    field_block = from_chunks(exchange(states_timed[None])[0])

    fine_end, decay = fine_solve(field_block, width, rows + 3 * width)
    timed = exchange(jnp.stack([cells_of(decay), cells_of(fine_end)]))
    offset_timed = timed[1] - timed[0] * strip_timed
    states_timed = scan_over_time(timed[0], offset_timed)
    ends_timed = timed[1]
    jumps_timed = jnp.concatenate([ends_timed[slices - 1 :], ends_timed[: slices - 1]], 0) - states_timed
    back = exchange(jnp.stack([states_timed, jumps_timed]))
    return (grid_of(back[0])[None], grid_of(back[1])[None])


def solution(mesh):
    placed = (P("tm", "space", None), P("space", None), P(None, "space", None), P())
    return jax.shard_map(
        on_device,
        mesh=mesh,
        in_specs=placed,
        out_specs=(P("tm", "space", None), P("tm", "space", None)),
        check_vma=False,
    )
```

```python
import math

import jax
import jax.numpy as jnp
from jax import lax
from jax.sharding import PartitionSpec as P

FINE = 16
ITERS = 2
SCAN_RADIX = 4


RELUCTIVITY = (1.0, 0.3, 1.0, 0.25)
SATURATION = (0.0, 2.0, 0.0, 1.5)
MOBILITY = (0.15, 0.02, 0.0004, 0.0008)


def with_halo(block, width):
    count = lax.axis_size("space")
    rows = block.shape[-2]
    forward = [(i, i + 1) for i in range(count - 1)]
    backward = [(i + 1, i) for i in range(count - 1)]
    above = lax.ppermute(lax.slice_in_dim(block, rows - width, rows, axis=block.ndim - 2), "space", forward)
    below = lax.ppermute(lax.slice_in_dim(block, 0, width, axis=block.ndim - 2), "space", backward)
    return jnp.concatenate([above, block, below], axis=block.ndim - 2)


def lookup_shifted(code, table):
    result = jnp.zeros(code.shape, jnp.float32)
    for region, entry_value in enumerate(table):
        result = result + jnp.where(code == jnp.float32(region + 1), jnp.float32(entry_value), jnp.float32(0.0))
    return result


def face_terms(values, axis):
    pad = [(0, 0)] * values.ndim
    pad[axis] = (1, 1)
    padded = jnp.pad(values, pad)
    n = padded.shape[axis]
    return 0.5 * (lax.slice_in_dim(padded, 0, n - 1, axis=axis) + lax.slice_in_dim(padded, 1, n, axis=axis))


def flux_terms(field, row_rel, row_sat, col_rel, col_sat):
    rows, cols = field.shape
    rpad = jnp.pad(field, ((1, 1), (0, 0)))
    row_diff = rpad[1:] - rpad[:-1]
    row_sq = row_diff * row_diff
    row_w = row_rel * (1.0 + row_sat * row_sq / (1.0 + row_sq))
    row_flux = row_w * row_diff
    cpad = jnp.pad(field, ((0, 0), (1, 1)))
    col_diff = cpad[:, 1:] - cpad[:, :-1]
    col_sq = col_diff * col_diff
    col_w = col_rel * (1.0 + col_sat * col_sq / (1.0 + col_sq))
    col_flux = col_w * col_diff
    divergence = (((-row_flux[:-1]) + row_flux[1:]) + (-col_flux[:, :-1])) + col_flux[:, 1:]
    diagonal = ((row_w[:-1] + row_w[1:]) + col_w[:, :-1]) + col_w[:, 1:]
    return divergence, diagonal


def neighbours(x):
    padded = jnp.pad(x, ((1, 1), (1, 1)))
    return (padded[:-2, 1:-1], padded[2:, 1:-1], padded[1:-1, :-2], padded[1:-1, 2:])


def neighbour_faces(reluctivity, saturation):
    rel_faces = [0.5 * (reluctivity + other) for other in neighbours(reluctivity)]
    sat_faces = [0.5 * (saturation + other) for other in neighbours(saturation)]
    return list(zip(rel_faces, sat_faces))


def cell_terms(field, faces):
    divergence = jnp.zeros_like(field)
    diagonal = jnp.zeros_like(field)
    for other, (face_rel, face_sat) in zip(neighbours(field), faces):
        difference = other - field
        square = difference * difference
        weight = face_rel * (1.0 + face_sat * square / (1.0 + square))
        divergence = divergence + weight * difference
        diagonal = diagonal + weight
    return divergence, diagonal


def compose_maps(earlier, later):
    return (later[0] * earlier[0], later[0] * earlier[1] + later[1])


def periodic_states(decay, offset, extra):
    count = lax.axis_size("tm")

    def from_behind(x, by):
        return lax.ppermute(x, "tm", [(i, (i + by) % count) for i in range(count)])

    own = jnp.stack([decay, offset])
    first = min(SCAN_RADIX, count)
    got = [from_behind(jnp.stack([decay, offset] + extra), 1)]
    got += [from_behind(own, by) for by in range(2, first + 1)]
    carried = [part[2:] for part in got[:1]]
    window = (got[-1][0], got[-1][1])
    for part in reversed(got[:-1]):
        window = compose_maps(window, (part[0], part[1]))
    length = first
    while length < count:
        parts = [from_behind(jnp.stack(window), by * length) for by in range(1, SCAN_RADIX) if by * length < count]
        joined = (parts[-1][0], parts[-1][1])
        for part in reversed(parts[:-1]):
            joined = compose_maps(joined, (part[0], part[1]))
        window = compose_maps(joined, window)
        length = length * (len(parts) + 1)
    return window[1], (carried[0] if extra else None)


def shift_down(x, by, fill):
    head = jnp.full(x.shape[:1] + (by,) + x.shape[2:], fill, x.dtype)
    return jnp.concatenate([head, x[:, : x.shape[1] - by]], axis=1)


def transposed_states(decay, offset, extra):
    count = lax.axis_size("tm")
    rows, cols = decay.shape
    parts = jnp.stack([decay, offset] + extra).reshape(2 + len(extra), count, rows * cols // count)
    cells = lax.all_to_all(parts, "tm", 1, 1, tiled=True)
    factor, shift = cells[0], cells[1]
    span = 1
    while span < count:
        earlier_factor = shift_down(factor[None], span, 1.0)[0]
        earlier_shift = shift_down(shift[None], span, 0.0)[0]
        factor, shift = factor * earlier_factor, factor * earlier_shift + shift
        span *= 2
    closing = shift[count - 1 :]
    before_factor = shift_down(factor[None], 1, 1.0)[0]
    before_shift = shift_down(shift[None], 1, 0.0)[0]
    states = before_factor * closing + before_shift
    outs = [states]
    if extra:
        ends = cells[2]
        outs.append(jnp.concatenate([ends[count - 1 :], ends[: count - 1]], axis=0) - states)
    back = lax.all_to_all(jnp.stack(outs), "tm", 1, 1, tiled=True)
    back = back.reshape(len(outs), rows, cols)
    return back[0], (back[1:] if extra else None)


def scan_over_time(factor, shift):
    count = factor.shape[0]
    span = 1
    while span < count:
        earlier_factor = shift_down(factor[None], span, 1.0)[0]
        earlier_shift = shift_down(shift[None], span, 0.0)[0]
        factor, shift = factor * earlier_factor, factor * earlier_shift + shift
        span *= 2
    closing = shift[count - 1 :]
    before_factor = shift_down(factor[None], 1, 1.0)[0]
    before_shift = shift_down(shift[None], 1, 0.0)[0]
    return before_factor * closing + before_shift


def exchange(parts):
    return lax.all_to_all(parts, "tm", 1, 1, tiled=True)


def on_device(start_states, region_map, source, front):
    field_now = start_states[0]
    rows, cols = field_now.shape
    width = FINE
    slices = lax.axis_size("tm")
    reach = 2 * FINE
    assert ITERS == 2 and reach <= rows and (rows * cols) % slices == 0 and (2 * width * cols) % slices == 0
    slice_index = lax.axis_index("tm")
    scale = 2.0 * math.pi / (slices * FINE)

    stacked = jnp.stack(
        [field_now, region_map.astype(jnp.float32) + 1.0, source[0], source[1]], 0
    )
    extended = with_halo(stacked, reach)
    code = extended[1]
    reluct = lookup_shifted(code, RELUCTIVITY)
    satur = lookup_shifted(code, SATURATION)
    mobile_all = lookup_shifted(code, MOBILITY)
    cos_all, sin_all = extended[2], extended[3]
    cut_slice = (front - 1) % slices
    keep_map = slice_index != cut_slice

    def fine_solve(values, low, high):
        faces = neighbour_faces(reluct[low:high], satur[low:high])
        mobile_ext = mobile_all[low:high]
        src_cos, src_sin = cos_all[low:high], sin_all[low:high]

        def single_step(values, step_index):
            divergence, diagonal = cell_terms(values, faces)
            phase_angle = (slice_index * FINE + step_index).astype(jnp.float32) * scale
            current = src_cos * jnp.cos(phase_angle) + src_sin * jnp.sin(phase_angle)
            return values + mobile_ext * (divergence + current), diagonal

        fine_values, fine_diagonal = single_step(values, 0)
        for step_index in range(1, FINE):
            fine_values = single_step(fine_values, step_index)[0]
        fine_values = fine_values[FINE : high - low - FINE]
        fine_diagonal = fine_diagonal[FINE : high - low - FINE]
        mobile = mobile_all[low + FINE : high - FINE]
        decay = 1.0 / (1.0 + FINE * mobile * fine_diagonal)
        return fine_values, jnp.where(keep_map, decay, 0.0)

    own_cells = rows * cols // slices
    assert rows % 8 == 0 and cols % 128 == 0 and (2 * width) % 8 == 0

    def cells_of(x):
        n = x.shape[0]
        return x.reshape(n // 8, 8, cols // 128, 128).transpose(0, 2, 1, 3).reshape(slices, -1)

    def grid_of(chunks):
        n = chunks.size // cols
        return chunks.reshape(n // 8, cols // 128, 8, 128).transpose(0, 2, 1, 3).reshape(n, cols)

    def to_chunks(block):
        own = cells_of(block[width : width + rows])
        halo = cells_of(jnp.concatenate([block[:width], block[width + rows :]], 0))
        return jnp.concatenate([own, halo], 1)

    def from_chunks(chunks):
        own = grid_of(chunks[:, :own_cells])
        halo = grid_of(chunks[:, own_cells:])
        return jnp.concatenate([halo[:width], own, halo[width:]], 0)

    fine_end, decay = fine_solve(extended[0], 0, rows + 2 * reach)
    offset = fine_end - decay * extended[0][width : width + rows + 2 * width]
    timed = exchange(jnp.stack([to_chunks(decay), to_chunks(offset)]))
    states_timed = scan_over_time(timed[0], timed[1])
    strip_timed = states_timed[:, :own_cells]
    field_block = from_chunks(exchange(states_timed[None])[0])

    fine_end, decay = fine_solve(field_block, width, rows + 3 * width)
    timed = exchange(jnp.stack([cells_of(decay), cells_of(fine_end)]))
    offset_timed = timed[1] - timed[0] * strip_timed
    states_timed = scan_over_time(timed[0], offset_timed)
    ends_timed = timed[1]
    jumps_timed = jnp.concatenate([ends_timed[slices - 1 :], ends_timed[: slices - 1]], 0) - states_timed
    back = exchange(jnp.stack([states_timed, jumps_timed]))
    return (grid_of(back[0])[None], grid_of(back[1])[None])


def solution(mesh):
    placed = (P("tm", "space", None), P("space", None), P(None, "space", None), P())
    return jax.shard_map(
        on_device,
        mesh=mesh,
        in_specs=placed,
        out_specs=(P("tm", "space", None), P("tm", "space", None)),
        check_vma=False,
    )
```

```python
import math

import jax
import jax.numpy as jnp
from jax import lax
from jax.sharding import PartitionSpec as P

FINE = 16
ITERS = 2
SCAN_RADIX = 4


RELUCTIVITY = (1.0, 0.3, 1.0, 0.25)
SATURATION = (0.0, 2.0, 0.0, 1.5)
MOBILITY = (0.15, 0.02, 0.0004, 0.0008)


def with_halo(block, width):
    count = lax.axis_size("space")
    rows = block.shape[-2]
    forward = [(i, i + 1) for i in range(count - 1)]
    backward = [(i + 1, i) for i in range(count - 1)]
    above = lax.ppermute(lax.slice_in_dim(block, rows - width, rows, axis=block.ndim - 2), "space", forward)
    below = lax.ppermute(lax.slice_in_dim(block, 0, width, axis=block.ndim - 2), "space", backward)
    return jnp.concatenate([above, block, below], axis=block.ndim - 2)


def lookup_shifted(code, table):
    result = jnp.zeros(code.shape, jnp.float32)
    for region, entry_value in enumerate(table):
        result = result + jnp.where(code == jnp.float32(region + 1), jnp.float32(entry_value), jnp.float32(0.0))
    return result


def face_terms(values, axis):
    pad = [(0, 0)] * values.ndim
    pad[axis] = (1, 1)
    padded = jnp.pad(values, pad)
    n = padded.shape[axis]
    return 0.5 * (lax.slice_in_dim(padded, 0, n - 1, axis=axis) + lax.slice_in_dim(padded, 1, n, axis=axis))


def flux_terms(field, row_rel, row_sat, col_rel, col_sat):
    rows, cols = field.shape
    rpad = jnp.pad(field, ((1, 1), (0, 0)))
    row_diff = rpad[1:] - rpad[:-1]
    row_sq = row_diff * row_diff
    row_w = row_rel * (1.0 + row_sat * row_sq / (1.0 + row_sq))
    row_flux = row_w * row_diff
    cpad = jnp.pad(field, ((0, 0), (1, 1)))
    col_diff = cpad[:, 1:] - cpad[:, :-1]
    col_sq = col_diff * col_diff
    col_w = col_rel * (1.0 + col_sat * col_sq / (1.0 + col_sq))
    col_flux = col_w * col_diff
    divergence = (((-row_flux[:-1]) + row_flux[1:]) + (-col_flux[:, :-1])) + col_flux[:, 1:]
    diagonal = ((row_w[:-1] + row_w[1:]) + col_w[:, :-1]) + col_w[:, 1:]
    return divergence, diagonal


def neighbours(x):
    padded = jnp.pad(x, ((1, 1), (1, 1)))
    return (padded[:-2, 1:-1], padded[2:, 1:-1], padded[1:-1, :-2], padded[1:-1, 2:])


def neighbour_faces(reluctivity, saturation):
    rel_faces = [0.5 * (reluctivity + other) for other in neighbours(reluctivity)]
    sat_faces = [0.5 * (saturation + other) for other in neighbours(saturation)]
    return list(zip(rel_faces, sat_faces))


def cell_terms(field, faces):
    divergence = jnp.zeros_like(field)
    diagonal = jnp.zeros_like(field)
    for other, (face_rel, face_sat) in zip(neighbours(field), faces):
        difference = other - field
        square = difference * difference
        weight = face_rel * (1.0 + face_sat * square / (1.0 + square))
        divergence = divergence + weight * difference
        diagonal = diagonal + weight
    return divergence, diagonal


def compose_maps(earlier, later):
    return (later[0] * earlier[0], later[0] * earlier[1] + later[1])


def periodic_states(decay, offset, extra):
    count = lax.axis_size("tm")

    def from_behind(x, by):
        return lax.ppermute(x, "tm", [(i, (i + by) % count) for i in range(count)])

    own = jnp.stack([decay, offset])
    first = min(SCAN_RADIX, count)
    got = [from_behind(jnp.stack([decay, offset] + extra), 1)]
    got += [from_behind(own, by) for by in range(2, first + 1)]
    carried = [part[2:] for part in got[:1]]
    window = (got[-1][0], got[-1][1])
    for part in reversed(got[:-1]):
        window = compose_maps(window, (part[0], part[1]))
    length = first
    while length < count:
        parts = [from_behind(jnp.stack(window), by * length) for by in range(1, SCAN_RADIX) if by * length < count]
        joined = (parts[-1][0], parts[-1][1])
        for part in reversed(parts[:-1]):
            joined = compose_maps(joined, (part[0], part[1]))
        window = compose_maps(joined, window)
        length = length * (len(parts) + 1)
    return window[1], (carried[0] if extra else None)


def shift_down(x, by, fill):
    head = jnp.full(x.shape[:1] + (by,) + x.shape[2:], fill, x.dtype)
    return jnp.concatenate([head, x[:, : x.shape[1] - by]], axis=1)


def transposed_states(decay, offset, extra):
    count = lax.axis_size("tm")
    rows, cols = decay.shape
    parts = jnp.stack([decay, offset] + extra).reshape(2 + len(extra), count, rows * cols // count)
    cells = lax.all_to_all(parts, "tm", 1, 1, tiled=True)
    factor, shift = cells[0], cells[1]
    span = 1
    while span < count:
        earlier_factor = shift_down(factor[None], span, 1.0)[0]
        earlier_shift = shift_down(shift[None], span, 0.0)[0]
        factor, shift = factor * earlier_factor, factor * earlier_shift + shift
        span *= 2
    closing = shift[count - 1 :]
    before_factor = shift_down(factor[None], 1, 1.0)[0]
    before_shift = shift_down(shift[None], 1, 0.0)[0]
    states = before_factor * closing + before_shift
    outs = [states]
    if extra:
        ends = cells[2]
        outs.append(jnp.concatenate([ends[count - 1 :], ends[: count - 1]], axis=0) - states)
    back = lax.all_to_all(jnp.stack(outs), "tm", 1, 1, tiled=True)
    back = back.reshape(len(outs), rows, cols)
    return back[0], (back[1:] if extra else None)


def scan_over_time(factor, shift):
    count = factor.shape[0]
    span = 1
    while span < count:
        earlier_factor = shift_down(factor[None], span, 1.0)[0]
        earlier_shift = shift_down(shift[None], span, 0.0)[0]
        factor, shift = factor * earlier_factor, factor * earlier_shift + shift
        span *= 2
    closing = shift[count - 1 :]
    before_factor = shift_down(factor[None], 1, 1.0)[0]
    before_shift = shift_down(shift[None], 1, 0.0)[0]
    return before_factor * closing + before_shift


def exchange(parts):
    return lax.all_to_all(parts, "tm", 1, 1, tiled=True)


def on_device(start_states, region_map, source, front):
    field_now = start_states[0]
    rows, cols = field_now.shape
    width = FINE
    slices = lax.axis_size("tm")
    reach = 2 * FINE
    assert ITERS == 2 and reach <= rows and (rows * cols) % slices == 0 and (2 * width * cols) % slices == 0
    slice_index = lax.axis_index("tm")
    scale = 2.0 * math.pi / (slices * FINE)

    stacked = jnp.stack(
        [field_now, region_map.astype(jnp.float32) + 1.0, source[0], source[1]], 0
    )
    extended = with_halo(stacked, reach)
    code = extended[1]
    reluct = lookup_shifted(code, RELUCTIVITY)
    satur = lookup_shifted(code, SATURATION)
    mobile_all = lookup_shifted(code, MOBILITY)
    cos_all, sin_all = extended[2], extended[3]
    cut_slice = (front - 1) % slices
    keep_map = slice_index != cut_slice

    def fine_solve(values, low, high):
        def single_step(values, step_index, trim):
            window = slice(low + trim, high - trim)
            faces = neighbour_faces(reluct[window], satur[window])
            divergence, diagonal = cell_terms(values, faces)
            phase_angle = (slice_index * FINE + step_index).astype(jnp.float32) * scale
            current = cos_all[window] * jnp.cos(phase_angle) + sin_all[window] * jnp.sin(phase_angle)
            return values + mobile_all[window] * (divergence + current), diagonal

        fine_values, fine_diagonal = single_step(values, 0, 0)
        trim = 0
        for step_index in range(1, FINE):
            if step_index >= trim + 8:
                trim += 8
                fine_values = fine_values[8:-8]
            fine_values = single_step(fine_values, step_index, trim)[0]
        fine_values = fine_values[FINE - trim : high - low - FINE - trim]
        fine_diagonal = fine_diagonal[FINE : high - low - FINE]
        mobile = mobile_all[low + FINE : high - FINE]
        decay = 1.0 / (1.0 + FINE * mobile * fine_diagonal)
        return fine_values, jnp.where(keep_map, decay, 0.0)

    own_cells = rows * cols // slices
    assert rows % 8 == 0 and cols % 128 == 0 and (2 * width) % 8 == 0

    def cells_of(x):
        n = x.shape[0]
        return x.reshape(n // 8, 8, cols // 128, 128).transpose(0, 2, 1, 3).reshape(slices, -1)

    def grid_of(chunks):
        n = chunks.size // cols
        return chunks.reshape(n // 8, cols // 128, 8, 128).transpose(0, 2, 1, 3).reshape(n, cols)

    def to_chunks(block):
        own = cells_of(block[width : width + rows])
        halo = cells_of(jnp.concatenate([block[:width], block[width + rows :]], 0))
        return jnp.concatenate([own, halo], 1)

    def from_chunks(chunks):
        own = grid_of(chunks[:, :own_cells])
        halo = grid_of(chunks[:, own_cells:])
        return jnp.concatenate([halo[:width], own, halo[width:]], 0)

    fine_end, decay = fine_solve(extended[0], 0, rows + 2 * reach)
    offset = fine_end - decay * extended[0][width : width + rows + 2 * width]
    timed = exchange(jnp.stack([to_chunks(decay), to_chunks(offset)]))
    states_timed = scan_over_time(timed[0], timed[1])
    strip_timed = states_timed[:, :own_cells]
    field_block = from_chunks(exchange(states_timed[None])[0])

    fine_end, decay = fine_solve(field_block, width, rows + 3 * width)
    timed = exchange(jnp.stack([cells_of(decay), cells_of(fine_end)]))
    offset_timed = timed[1] - timed[0] * strip_timed
    states_timed = scan_over_time(timed[0], offset_timed)
    ends_timed = timed[1]
    jumps_timed = jnp.concatenate([ends_timed[slices - 1 :], ends_timed[: slices - 1]], 0) - states_timed
    back = exchange(jnp.stack([states_timed, jumps_timed]))
    return (grid_of(back[0])[None], grid_of(back[1])[None])


def solution(mesh):
    placed = (P("tm", "space", None), P("space", None), P(None, "space", None), P())
    return jax.shard_map(
        on_device,
        mesh=mesh,
        in_specs=placed,
        out_specs=(P("tm", "space", None), P("tm", "space", None)),
        check_vma=False,
    )
```

```python
import math

import jax
import jax.numpy as jnp
from jax import lax
from jax.sharding import PartitionSpec as P

FINE = 16
ITERS = 2
SCAN_RADIX = 4


RELUCTIVITY = (1.0, 0.3, 1.0, 0.25)
SATURATION = (0.0, 2.0, 0.0, 1.5)
MOBILITY = (0.15, 0.02, 0.0004, 0.0008)


def with_halo(block, width):
    count = lax.axis_size("space")
    rows = block.shape[-2]
    forward = [(i, i + 1) for i in range(count - 1)]
    backward = [(i + 1, i) for i in range(count - 1)]
    above = lax.ppermute(lax.slice_in_dim(block, rows - width, rows, axis=block.ndim - 2), "space", forward)
    below = lax.ppermute(lax.slice_in_dim(block, 0, width, axis=block.ndim - 2), "space", backward)
    return jnp.concatenate([above, block, below], axis=block.ndim - 2)


def lookup_shifted(code, table):
    result = jnp.zeros(code.shape, jnp.float32)
    for region, entry_value in enumerate(table):
        result = result + jnp.where(code == jnp.float32(region + 1), jnp.float32(entry_value), jnp.float32(0.0))
    return result


def face_terms(values, axis):
    pad = [(0, 0)] * values.ndim
    pad[axis] = (1, 1)
    padded = jnp.pad(values, pad)
    n = padded.shape[axis]
    return 0.5 * (lax.slice_in_dim(padded, 0, n - 1, axis=axis) + lax.slice_in_dim(padded, 1, n, axis=axis))


def flux_terms(field, row_rel, row_sat, col_rel, col_sat):
    rows, cols = field.shape
    rpad = jnp.pad(field, ((1, 1), (0, 0)))
    row_diff = rpad[1:] - rpad[:-1]
    row_sq = row_diff * row_diff
    row_w = row_rel * (1.0 + row_sat * row_sq / (1.0 + row_sq))
    row_flux = row_w * row_diff
    cpad = jnp.pad(field, ((0, 0), (1, 1)))
    col_diff = cpad[:, 1:] - cpad[:, :-1]
    col_sq = col_diff * col_diff
    col_w = col_rel * (1.0 + col_sat * col_sq / (1.0 + col_sq))
    col_flux = col_w * col_diff
    divergence = (((-row_flux[:-1]) + row_flux[1:]) + (-col_flux[:, :-1])) + col_flux[:, 1:]
    diagonal = ((row_w[:-1] + row_w[1:]) + col_w[:, :-1]) + col_w[:, 1:]
    return divergence, diagonal


def neighbours(x):
    padded = jnp.pad(x, ((1, 1), (1, 1)))
    return (padded[:-2, 1:-1], padded[2:, 1:-1], padded[1:-1, :-2], padded[1:-1, 2:])


def neighbour_faces(reluctivity, saturation):
    rel_faces = [0.5 * (reluctivity + other) for other in neighbours(reluctivity)]
    sat_faces = [0.5 * (saturation + other) for other in neighbours(saturation)]
    return list(zip(rel_faces, sat_faces))


def cell_terms(field, faces):
    divergence = jnp.zeros_like(field)
    diagonal = jnp.zeros_like(field)
    for other, (face_rel, face_sat) in zip(neighbours(field), faces):
        difference = other - field
        square = difference * difference
        weight = face_rel * (1.0 + face_sat * square / (1.0 + square))
        divergence = divergence + weight * difference
        diagonal = diagonal + weight
    return divergence, diagonal


def compose_maps(earlier, later):
    return (later[0] * earlier[0], later[0] * earlier[1] + later[1])


def periodic_states(decay, offset, extra):
    count = lax.axis_size("tm")

    def from_behind(x, by):
        return lax.ppermute(x, "tm", [(i, (i + by) % count) for i in range(count)])

    own = jnp.stack([decay, offset])
    first = min(SCAN_RADIX, count)
    got = [from_behind(jnp.stack([decay, offset] + extra), 1)]
    got += [from_behind(own, by) for by in range(2, first + 1)]
    carried = [part[2:] for part in got[:1]]
    window = (got[-1][0], got[-1][1])
    for part in reversed(got[:-1]):
        window = compose_maps(window, (part[0], part[1]))
    length = first
    while length < count:
        parts = [from_behind(jnp.stack(window), by * length) for by in range(1, SCAN_RADIX) if by * length < count]
        joined = (parts[-1][0], parts[-1][1])
        for part in reversed(parts[:-1]):
            joined = compose_maps(joined, (part[0], part[1]))
        window = compose_maps(joined, window)
        length = length * (len(parts) + 1)
    return window[1], (carried[0] if extra else None)


def shift_down(x, by, fill):
    head = jnp.full(x.shape[:1] + (by,) + x.shape[2:], fill, x.dtype)
    return jnp.concatenate([head, x[:, : x.shape[1] - by]], axis=1)


def transposed_states(decay, offset, extra):
    count = lax.axis_size("tm")
    rows, cols = decay.shape
    parts = jnp.stack([decay, offset] + extra).reshape(2 + len(extra), count, rows * cols // count)
    cells = lax.all_to_all(parts, "tm", 1, 1, tiled=True)
    factor, shift = cells[0], cells[1]
    span = 1
    while span < count:
        earlier_factor = shift_down(factor[None], span, 1.0)[0]
        earlier_shift = shift_down(shift[None], span, 0.0)[0]
        factor, shift = factor * earlier_factor, factor * earlier_shift + shift
        span *= 2
    closing = shift[count - 1 :]
    before_factor = shift_down(factor[None], 1, 1.0)[0]
    before_shift = shift_down(shift[None], 1, 0.0)[0]
    states = before_factor * closing + before_shift
    outs = [states]
    if extra:
        ends = cells[2]
        outs.append(jnp.concatenate([ends[count - 1 :], ends[: count - 1]], axis=0) - states)
    back = lax.all_to_all(jnp.stack(outs), "tm", 1, 1, tiled=True)
    back = back.reshape(len(outs), rows, cols)
    return back[0], (back[1:] if extra else None)


def scan_over_time(factor, shift):
    count = factor.shape[0]
    span = 1
    while span < count:
        earlier_factor = shift_down(factor[None], span, 1.0)[0]
        earlier_shift = shift_down(shift[None], span, 0.0)[0]
        factor, shift = factor * earlier_factor, factor * earlier_shift + shift
        span *= 2
    closing = shift[count - 1 :]
    before_factor = shift_down(factor[None], 1, 1.0)[0]
    before_shift = shift_down(shift[None], 1, 0.0)[0]
    return before_factor * closing + before_shift


def exchange(parts):
    return lax.all_to_all(parts, "tm", 1, 1, tiled=True)


def on_device(start_states, region_map, source, front):
    field_now = start_states[0]
    rows, cols = field_now.shape
    width = FINE
    slices = lax.axis_size("tm")
    reach = 2 * FINE
    assert ITERS == 2 and reach <= rows and (rows * cols) % slices == 0 and (2 * width * cols) % slices == 0
    slice_index = lax.axis_index("tm")
    scale = 2.0 * math.pi / (slices * FINE)

    stacked = jnp.stack(
        [field_now, region_map.astype(jnp.float32) + 1.0, source[0], source[1]], 0
    )
    extended = with_halo(stacked, reach)
    code = extended[1]
    reluct = lookup_shifted(code, RELUCTIVITY)
    satur = lookup_shifted(code, SATURATION)
    mobile_all = lookup_shifted(code, MOBILITY)
    cos_all, sin_all = extended[2], extended[3]
    cut_slice = (front - 1) % slices
    keep_map = slice_index != cut_slice

    def fine_solve(values, low, high):
        faces = neighbour_faces(reluct[low:high], satur[low:high])
        mobile_ext = mobile_all[low:high]
        src_cos, src_sin = cos_all[low:high], sin_all[low:high]

        def single_step(values, step_index):
            divergence, diagonal = cell_terms(values, faces)
            phase_angle = (slice_index * FINE + step_index).astype(jnp.float32) * scale
            current = src_cos * jnp.cos(phase_angle) + src_sin * jnp.sin(phase_angle)
            return values + mobile_ext * (divergence + current), diagonal

        fine_values, fine_diagonal = single_step(values, 0)
        for step_index in range(1, FINE):
            fine_values = single_step(fine_values, step_index)[0]
        fine_values = fine_values[FINE : high - low - FINE]
        fine_diagonal = fine_diagonal[FINE : high - low - FINE]
        mobile = mobile_all[low + FINE : high - FINE]
        decay = 1.0 / (1.0 + FINE * mobile * fine_diagonal)
        return fine_values, jnp.where(keep_map, decay, 0.0)

    own_cells = rows * cols // slices
    assert rows % 8 == 0 and cols % 128 == 0 and (2 * width) % 8 == 0

    def cells_of(x):
        n = x.shape[0]
        return x.reshape(n // 8, 8, cols // 128, 128).transpose(0, 2, 1, 3).reshape(slices, -1)

    def grid_of(chunks):
        n = chunks.size // cols
        return chunks.reshape(n // 8, cols // 128, 8, 128).transpose(0, 2, 1, 3).reshape(n, cols)

    def to_chunks(block):
        own = cells_of(block[width : width + rows])
        halo = cells_of(jnp.concatenate([block[:width], block[width + rows :]], 0))
        return jnp.concatenate([own, halo], 1)

    def from_chunks(chunks):
        own = grid_of(chunks[:, :own_cells])
        halo = grid_of(chunks[:, own_cells:])
        return jnp.concatenate([halo[:width], own, halo[width:]], 0)

    fine_end, decay = fine_solve(extended[0], 0, rows + 2 * reach)
    offset = fine_end - decay * extended[0][width : width + rows + 2 * width]
    timed = exchange(jnp.stack([to_chunks(decay), to_chunks(offset)]))
    states_timed = scan_over_time(timed[0], timed[1])
    strip_timed = states_timed[:, :own_cells]
    field_block = from_chunks(exchange(states_timed[None])[0])

    fine_end, decay = fine_solve(field_block, width, rows + 3 * width)
    previous_end = lax.ppermute(fine_end, "tm", [(i, (i + 1) % slices) for i in range(slices)])
    timed = exchange(jnp.stack([cells_of(decay), cells_of(fine_end)]))
    offset_timed = timed[1] - timed[0] * strip_timed
    states_timed = scan_over_time(timed[0], offset_timed)
    states = grid_of(lax.all_to_all(states_timed, "tm", 0, 0, tiled=True))
    return (states[None], (previous_end - states)[None])


def solution(mesh):
    placed = (P("tm", "space", None), P("space", None), P(None, "space", None), P())
    return jax.shard_map(
        on_device,
        mesh=mesh,
        in_specs=placed,
        out_specs=(P("tm", "space", None), P("tm", "space", None)),
        check_vma=False,
    )
```
